256 devices in a mesh: member: 4 (over x), fsdp: 64 (over z, y, core).
Axes of the slice: x: 4, y: 4, z: 8, core: 2. Of those that a mesh axis runs over, the one named last changes fastest.
Arguments:
- query_rows: bfloat16 [65536, 2560], P(('member', 'fsdp')), parts along dimension 0, may hold values from -110 to 110
- key_rows: bfloat16 [65536, 2560], P(('member', 'fsdp')), parts along dimension 0, may hold values from -9 to 9
- value_rows: bfloat16 [65536, 2560], P(('member', 'fsdp')), parts along dimension 0, may hold values from -24 to 24
- weight_out: bfloat16 [10240, 2560], P(('member', 'fsdp')), parts along dimension 0, may hold values from -0.125 to 0.125
- cotangent: bfloat16 [65536, 2560], P(('member', 'fsdp')), parts along dimension 0, may hold values from -24 to 24
- pattern: int32 [64, 16, 6], P('member'), parts along dimension 0, may hold values from 0 to 15, as said below
Outputs:
- sublayer_out: bfloat16 [65536, 2560], P(('member', 'fsdp')), parts along dimension 0
- grad_queries: bfloat16 [65536, 2560], P(('member', 'fsdp')), parts along dimension 0
- grad_keys: bfloat16 [65536, 2560], P(('member', 'fsdp')), parts along dimension 0
- grad_values: bfloat16 [65536, 2560], P(('member', 'fsdp')), parts along dimension 0
The draws below stay inside these ranges and needn't reach their ends.
There are 4 independent parts, one for each index of `member`. The reference program is written for one: setup_inputs(seed, part) draws one part's arguments, and reference() takes and returns one part's arrays. A program takes and returns all parts, laid end to end along the dimension named above; each array names one. Nothing has to cross between parts.
Inputs may be any that keep to these rules, and one draw needn't show every extreme that they name: `pattern`: for each sequence and query block b the 6 entries are distinct key blocks of the same sequence; they include b, b - 1 and b + 1 where these exist and block 0, and the others are random.
All inputs are finite; a program needn't handle non-finite values.
Results may differ from the reference program's by a relative error of at most 0.035.
Values may be sent and summed in bfloat16 or wider, within the bound.
No kernel may reach another device: no remote copies, remote signals or barrier semaphores. Data moves between devices by JAX's collectives and lax.ppermute only.
A program may use at most 192 MiB of HBM per device.

```python
import math
import jax
import jax.numpy as jnp
from jax import lax

D = 2560
HEADS = 20
HSIZE = 128
HD = 2560
BLK = 64
QBLK = 16
NSEL = 6
TOK_DEV = 256
LEN = 1024
TOKENS = 16384
SEQS = 16


def paired_rows(key):
    base_keys = jax.random.truncated_normal(jax.random.fold_in(key, 101), -4.0, 4.0, (TOKENS, HD), jnp.float32)
    base_queries = jax.random.truncated_normal(jax.random.fold_in(key, 102), -4.0, 4.0, (TOKENS, HD), jnp.float32)
    return (base_queries, base_keys)


def draw_query_rows(key, part):
    return paired_rows(key)[0].astype(jnp.bfloat16)


def draw_key_rows(key, part):
    return paired_rows(key)[1].astype(jnp.bfloat16)


def draw_pattern(key, part):
    blocks = jnp.arange(QBLK, dtype=jnp.int32)
    query_blk = blocks[None, :, None]
    key_blk = blocks[None, None, :]
    forced = (key_blk == query_blk) | (key_blk == query_blk - 1) | (key_blk == query_blk + 1) | (key_blk == 0)
    noise_int = jax.random.randint(key, (SEQS, QBLK, QBLK), 0, 1 << 20, jnp.int32)
    scores = forced.astype(jnp.int32) * (1 << 26) + noise_int * QBLK + key_blk
    picked = lax.top_k(scores, NSEL)[1]
    return picked.astype(jnp.int32)


def levels(key, shape, pieces, smallest, top_value):
    level = 1.0
    for axis_at, parts in pieces:
        heights = jax.random.uniform(jax.random.fold_in(jax.random.fold_in(key, 6), axis_at), (parts,), jnp.float32, smallest / len(pieces), top_value / len(pieces))
        level = level * jnp.repeat(jnp.exp(heights), shape[axis_at] // parts).reshape((-1,) + (1,) * (len(shape) - 1 - axis_at))
    return level


def bell_draw(key, extent, deviation, most, shards=(), kind=jnp.bfloat16):
    array = jax.random.normal(key, extent, jnp.float32) * deviation
    if len(shards) > 0:
        array = levels(key, extent, shards, -0.22, 0.18) * array
    return jnp.clip(array, min=-most, max=most).astype(kind)


def setup_inputs(seed: int = 0, part: int = 0) -> dict:
    key_of = jax.random.split(jax.random.key(seed), 7)
    part_keys = jax.random.split(jax.random.fold_in(key_of[6], part), 7)
    return {
        "query_rows": draw_query_rows(jax.random.fold_in(jax.random.fold_in(key_of[6], part), 71), part),
        "key_rows": draw_key_rows(jax.random.fold_in(jax.random.fold_in(key_of[6], part), 71), part),
        "value_rows": bell_draw(part_keys[2], (TOKENS, HD), 4.0, 24.0, ((0, 64),)),
        "weight_out": bell_draw(part_keys[3], (HD, D), HD ** -0.5, 0.125, ((0, 64),)),
        "cotangent": bell_draw(part_keys[4], (TOKENS, D), 4.0, 24.0, ((0, 64),)),
        "pattern": draw_pattern(jax.random.fold_in(jax.random.fold_in(key_of[6], part), 71), part),
    }


def reference(query_rows, key_rows, value_rows, weight_out, cotangent, pattern):
    scaling = 1.0 / math.sqrt(HSIZE)
    groups = LEN // TOK_DEV
    blocks_here = TOK_DEV // BLK
    grad_context = jnp.dot(cotangent, weight_out.T, preferred_element_type=jnp.float32).astype(jnp.bfloat16)

    def one_sequence(packed):
        seq_queries, seq_keys, seq_values, seq_grads, seq_plan = packed
        query_blk = seq_queries.astype(jnp.float32).reshape(QBLK, BLK, HEADS, HSIZE)
        grad_blk = seq_grads.astype(jnp.float32).reshape(QBLK, BLK, HEADS, HSIZE)
        key_sel = jnp.take(seq_keys.reshape(QBLK, BLK, HD), seq_plan, axis=0).astype(jnp.float32)
        key_sel = key_sel.reshape(QBLK, NSEL * BLK, HEADS, HSIZE)
        value_sel = jnp.take(seq_values.reshape(QBLK, BLK, HD), seq_plan, axis=0).astype(jnp.float32)
        value_sel = value_sel.reshape(QBLK, NSEL * BLK, HEADS, HSIZE)
        scores = jnp.einsum('bqhe,bkhe->bhqk', query_blk, key_sel) * scaling
        row_peak = lax.optimization_barrier(jnp.max(scores, axis=-1, keepdims=True))
        log_total = row_peak + jnp.log(lax.optimization_barrier(jnp.sum(jnp.exp(scores - row_peak), axis=-1, keepdims=True)))
        probs = jnp.exp(scores - log_total)
        probs_low = lax.optimization_barrier(probs.astype(jnp.bfloat16)).astype(jnp.float32)
        context = lax.optimization_barrier(jnp.einsum('bhqk,bkhe->bqhe', probs_low, value_sel).astype(jnp.bfloat16))
        grad_prob = jnp.einsum('bqhe,bkhe->bhqk', grad_blk, value_sel)
        row_delta = jnp.einsum('bqhe,bqhe->bhq', grad_blk, context.astype(jnp.float32))
        grad_score = lax.optimization_barrier((probs * (grad_prob - row_delta[..., None])).astype(jnp.bfloat16))
        grad_score = grad_score.astype(jnp.float32)
        grad_queries = (jnp.einsum('bhqk,bkhe->bqhe', grad_score, key_sel) * scaling).astype(jnp.bfloat16)
        key_contrib = jnp.einsum('bhqk,bqhe->bkhe', grad_score, query_blk) * scaling
        value_contrib = jnp.einsum('bhqk,bqhe->bkhe', probs_low, grad_blk)
        onehot = (seq_plan[:, :, None] == jnp.arange(QBLK, dtype=jnp.int32)[None, None, :]).astype(jnp.float32)
        onehot = onehot.reshape(groups, blocks_here, NSEL, QBLK)

        def owner_sum(contrib):
            grouped = contrib.reshape(groups, blocks_here, NSEL, BLK * HD)
            parts_f = jnp.einsum('gpsk,gpsr->gkr', onehot, grouped, precision=lax.Precision.HIGHEST)
            rounded = lax.optimization_barrier(parts_f.astype(jnp.bfloat16)).astype(jnp.float32)
            return lax.optimization_barrier(jnp.sum(rounded, axis=0)).astype(jnp.bfloat16).reshape(LEN, HD)
        return (context.reshape(LEN, HD), grad_queries.reshape(LEN, HD), owner_sum(key_contrib), owner_sum(value_contrib))
    packed = (query_rows.reshape(SEQS, LEN, HD), key_rows.reshape(SEQS, LEN, HD), value_rows.reshape(SEQS, LEN, HD), grad_context.reshape(SEQS, LEN, HD), pattern)
    contexts, grad_q, grad_k, grad_v = lax.map(one_sequence, packed)
    context_all = contexts.reshape(TOKENS, HD)
    sublayer_out = jnp.dot(context_all, weight_out, preferred_element_type=jnp.float32).astype(jnp.bfloat16)
    return (sublayer_out, grad_q.reshape(TOKENS, HD), grad_k.reshape(TOKENS, HD), grad_v.reshape(TOKENS, HD))
```

```python
import math

import jax
import jax.numpy as jnp
from jax import lax
from jax.experimental import pallas as pl
from jax.experimental.pallas import tpu as pltpu
from jax.sharding import Mesh
from jax.sharding import PartitionSpec as P

HEADS = 20
HSIZE = 128
BLK = 64
QBLK = 16
NSEL = 6
LEN = 1024

SLOT_XOR = (0, 2, 1, 3)


def attn_kernel(q_ref, k0, k1, k2, k3, v0, v1, v2, v3, do_ref, mask_ref,
                ctx_ref, dq_ref, dk_ref, dv_ref):
    scaling = 1.0 / math.sqrt(HSIZE)
    q = q_ref[...]
    k = jnp.concatenate([k0[...], k1[...], k2[...], k3[...]], axis=0)
    v = jnp.concatenate([v0[...], v1[...], v2[...], v3[...]], axis=0)
    nt = (((1,), (1,)), ((), ()))
    tn = (((0,), (0,)), ((), ()))
    s = lax.dot_general(q, k, nt, preferred_element_type=jnp.float32) * scaling
    s = jnp.where(mask_ref[...] > 0, s, -jnp.inf)
    m = jnp.max(s, axis=1, keepdims=True)
    total = jnp.sum(jnp.exp(s - m), axis=1, keepdims=True)
    lse = m + jnp.log(total)
    p = jnp.exp(s - lse)
    p_low = p.astype(jnp.bfloat16)
    ctx = jnp.dot(p_low, v, preferred_element_type=jnp.float32).astype(jnp.bfloat16)
    ctx_ref[...] = ctx
    do = do_ref[...]
    dp = lax.dot_general(do, v, nt, preferred_element_type=jnp.float32)
    delta = jnp.sum(do.astype(jnp.float32) * ctx.astype(jnp.float32), axis=1, keepdims=True)
    ds = (p * (dp - delta)).astype(jnp.bfloat16)
    dq = jnp.dot(ds, k, preferred_element_type=jnp.float32) * scaling
    dq_ref[...] = dq.astype(jnp.bfloat16)
    dk = lax.dot_general(ds, q, tn, preferred_element_type=jnp.float32) * scaling
    dv = lax.dot_general(p_low, do, tn, preferred_element_type=jnp.float32)
    dk_ref[...] = dk.astype(jnp.bfloat16).reshape(dk_ref.shape)
    dv_ref[...] = dv.astype(jnp.bfloat16).reshape(dv_ref.shape)


def attention(q, ks, vs, do, mask):
    rows, width = q.shape
    keys = mask.shape[1]
    col = pl.BlockSpec((rows, HSIZE), lambda h: (0, h))
    slot_col = pl.BlockSpec((4, rows, HSIZE), lambda h: (0, 0, h))
    return pl.pallas_call(
        attn_kernel,
        grid=(width // HSIZE,),
        in_specs=[col] * 9 + [col, pl.BlockSpec((rows, keys), lambda h: (0, 0))],
        out_specs=[col, col, slot_col, slot_col],
        out_shape=[
            jax.ShapeDtypeStruct((rows, width), jnp.bfloat16),
            jax.ShapeDtypeStruct((rows, width), jnp.bfloat16),
            jax.ShapeDtypeStruct((4, rows, width), jnp.bfloat16),
            jax.ShapeDtypeStruct((4, rows, width), jnp.bfloat16),
        ],
    )(q, *ks, *vs, do, mask)


def swap(x, axis):
    count = lax.axis_size(axis)
    return lax.ppermute(x, axis, [(i, i ^ 1) for i in range(count)])


def per_device(query_rows, key_rows, value_rows, weight_out, cotangent, pattern):
    tok_rows = query_rows.shape[0]
    blocks_here = tok_rows // BLK
    chip = lax.axis_index("chip")
    core = lax.axis_index("core")
    seq_shards = LEN // tok_rows
    position = (chip % 2) * 2 + core
    sequence = chip // 2

    w_chip = lax.all_gather(weight_out, "chip", axis=0, tiled=False)
    w_full = lax.all_gather(w_chip, "core", axis=1, tiled=False)
    full_weight = w_full.reshape(-1, weight_out.shape[1])

    k_x = swap(key_rows, "chip")
    v_x = swap(value_rows, "chip")
    k_p = swap(key_rows, "core")
    v_p = swap(value_rows, "core")
    k_d = swap(k_x, "core")
    v_d = swap(v_x, "core")

    seq_plan = lax.dynamic_index_in_dim(pattern, sequence, 0, keepdims=False)
    own_plan = lax.dynamic_slice_in_dim(seq_plan, position * blocks_here, blocks_here, 0)
    rel = jnp.arange(seq_shards * blocks_here, dtype=jnp.int32)
    slot_xor = jnp.array(SLOT_XOR, dtype=jnp.int32)[rel // blocks_here]
    key_block = (position ^ slot_xor) * blocks_here + rel % blocks_here
    block_mask = jnp.any(own_plan[:, :, None] == key_block[None, None, :], axis=1)
    mask = jnp.broadcast_to(
        block_mask.astype(jnp.float32)[:, None, :, None],
        (blocks_here, BLK, seq_shards * blocks_here, BLK),
    ).reshape(tok_rows, seq_shards * tok_rows)

    grad_context = lax.dot_general(
        cotangent, full_weight, (((1,), (1,)), ((), ())), preferred_element_type=jnp.float32
    ).astype(jnp.bfloat16)

    ctx, grad_queries, dk, dv = attention(
        query_rows, (key_rows, k_x, k_p, k_d), (value_rows, v_x, v_p, v_d), grad_context, mask
    )
    sublayer_out = jnp.dot(ctx, full_weight, preferred_element_type=jnp.float32).astype(
        jnp.bfloat16
    )

    def reduce_parts(parts):
        back = swap(parts[2:4], "core")
        own = parts[0].astype(jnp.float32) + back[0].astype(jnp.float32)
        cross = (parts[1].astype(jnp.float32) + back[1].astype(jnp.float32)).astype(jnp.bfloat16)
        arrived = swap(cross, "chip")
        return (own + arrived.astype(jnp.float32)).astype(jnp.bfloat16)

    grad_keys = reduce_parts(dk)
    grad_values = reduce_parts(dv)
    return (sublayer_out, grad_queries, grad_keys, grad_values)


def solution(mesh):
    devices = mesh.devices.reshape(mesh.devices.shape[0], -1, 2)
    split = Mesh(devices, ("member", "chip", "core"))
    rows = P(("member", "chip", "core"), None)
    return jax.shard_map(
        per_device,
        mesh=split,
        in_specs=(rows, rows, rows, rows, rows, P("member", None, None)),
        out_specs=(rows, rows, rows, rows),
        check_vma=False,
    )
```

```python
import math

import jax
import jax.numpy as jnp
from jax import lax
from jax.experimental import pallas as pl
from jax.experimental.pallas import tpu as pltpu
from jax.sharding import Mesh
from jax.sharding import PartitionSpec as P

HEADS = 20
HSIZE = 128
BLK = 64
QBLK = 16
NSEL = 6
LEN = 1024

SLOT_XOR = (0, 2, 1, 3)


def masked_scores(q, k, mask):
    scaling = 1.0 / math.sqrt(HSIZE)
    nt = (((1,), (1,)), ((), ()))
    s = lax.dot_general(q, k, nt, preferred_element_type=jnp.float32) * scaling
    return jnp.where(mask > 0, s, -jnp.inf)


def fwd_kernel(q_ref, k0, k1, k2, k3, v0, v1, v2, v3, mask_ref, ctx_ref, lse_ref):
    q = q_ref[...]
    k = jnp.concatenate([k0[...], k1[...], k2[...], k3[...]], axis=0)
    v = jnp.concatenate([v0[...], v1[...], v2[...], v3[...]], axis=0)
    s = masked_scores(q, k, mask_ref[...])
    m = jnp.max(s, axis=1, keepdims=True)
    total = jnp.sum(jnp.exp(s - m), axis=1, keepdims=True)
    lse = m + jnp.log(total)
    p_low = jnp.exp(s - lse).astype(jnp.bfloat16)
    ctx_ref[...] = jnp.dot(p_low, v, preferred_element_type=jnp.float32).astype(jnp.bfloat16)
    lse_ref[...] = lse.reshape(lse_ref.shape)


def bwd_kernel(q_ref, k0, k1, k2, k3, v0, v1, v2, v3, do_ref, ctx_ref, lse_ref, mask_ref,
               dq_ref, dk_ref, dv_ref):
    scaling = 1.0 / math.sqrt(HSIZE)
    nt = (((1,), (1,)), ((), ()))
    tn = (((0,), (0,)), ((), ()))
    q = q_ref[...]
    k = jnp.concatenate([k0[...], k1[...], k2[...], k3[...]], axis=0)
    v = jnp.concatenate([v0[...], v1[...], v2[...], v3[...]], axis=0)
    s = masked_scores(q, k, mask_ref[...])
    lse = lse_ref[...].reshape(s.shape[0], 1)
    p = jnp.exp(s - lse)
    p_low = p.astype(jnp.bfloat16)
    do = do_ref[...]
    dp = lax.dot_general(do, v, nt, preferred_element_type=jnp.float32)
    delta = jnp.sum(
        do.astype(jnp.float32) * ctx_ref[...].astype(jnp.float32), axis=1, keepdims=True
    )
    ds = (p * (dp - delta)).astype(jnp.bfloat16)
    dq = jnp.dot(ds, k, preferred_element_type=jnp.float32) * scaling
    dq_ref[...] = dq.astype(jnp.bfloat16)
    dk = lax.dot_general(ds, q, tn, preferred_element_type=jnp.float32) * scaling
    dv = lax.dot_general(p_low, do, tn, preferred_element_type=jnp.float32)
    dk_ref[...] = dk.astype(jnp.bfloat16).reshape(dk_ref.shape)
    dv_ref[...] = dv.astype(jnp.bfloat16).reshape(dv_ref.shape)


def attention_fwd(q, ks, vs, mask):
    rows, width = q.shape
    heads = width // HSIZE
    col = pl.BlockSpec((rows, HSIZE), lambda h: (0, h))
    return pl.pallas_call(
        fwd_kernel,
        grid=(heads,),
        in_specs=[col] * 9 + [pl.BlockSpec(mask.shape, lambda h: (0, 0))],
        out_specs=[col, pl.BlockSpec((1, rows, 1), lambda h: (h, 0, 0))],
        out_shape=[
            jax.ShapeDtypeStruct((rows, width), jnp.bfloat16),
            jax.ShapeDtypeStruct((heads, rows, 1), jnp.float32),
        ],
    )(q, *ks, *vs, mask)


def attention_bwd(q, ks, vs, do, ctx, lse, mask, first, count):
    rows, width = q.shape
    col = pl.BlockSpec((rows, HSIZE), lambda h: (0, h + first))
    out_col = pl.BlockSpec((rows, HSIZE), lambda h: (0, h))
    slot_col = pl.BlockSpec((4, rows, HSIZE), lambda h: (0, 0, h))
    return pl.pallas_call(
        bwd_kernel,
        grid=(count,),
        in_specs=[col] * 11
        + [
            pl.BlockSpec((1, rows, 1), lambda h: (h + first, 0, 0)),
            pl.BlockSpec(mask.shape, lambda h: (0, 0)),
        ],
        out_specs=[out_col, slot_col, slot_col],
        out_shape=[
            jax.ShapeDtypeStruct((rows, count * HSIZE), jnp.bfloat16),
            jax.ShapeDtypeStruct((4, rows, count * HSIZE), jnp.bfloat16),
            jax.ShapeDtypeStruct((4, rows, count * HSIZE), jnp.bfloat16),
        ],
    )(q, *ks, *vs, do, ctx, lse, mask)


def swap(x, axis):
    count = lax.axis_size(axis)
    return lax.ppermute(x, axis, [(i, i ^ 1) for i in range(count)])


def per_device(query_rows, key_rows, value_rows, weight_out, cotangent, pattern):
    tok_rows = query_rows.shape[0]
    blocks_here = tok_rows // BLK
    zpos = lax.axis_index("z")
    ypos = lax.axis_index("y")
    core = lax.axis_index("core")
    seq_shards = LEN // tok_rows
    position = (ypos % 2) * 2 + core
    sequence = zpos * (lax.axis_size("y") // 2) + ypos // 2

    full_weight = lax.all_gather(weight_out, ("z", "y", "core"), axis=0, tiled=True)

    k_x = swap(key_rows, "y")
    v_x = swap(value_rows, "y")
    k_p = swap(key_rows, "core")
    v_p = swap(value_rows, "core")
    k_d = swap(k_x, "core")
    v_d = swap(v_x, "core")

    seq_plan = lax.dynamic_index_in_dim(pattern, sequence, 0, keepdims=False)
    own_plan = lax.dynamic_slice_in_dim(seq_plan, position * blocks_here, blocks_here, 0)
    rel = jnp.arange(seq_shards * blocks_here, dtype=jnp.int32)
    slot_xor = jnp.array(SLOT_XOR, dtype=jnp.int32)[rel // blocks_here]
    key_block = (position ^ slot_xor) * blocks_here + rel % blocks_here
    block_mask = jnp.any(own_plan[:, :, None] == key_block[None, None, :], axis=1)
    mask = jnp.broadcast_to(
        block_mask.astype(jnp.float32)[:, None, :, None],
        (blocks_here, BLK, seq_shards * blocks_here, BLK),
    ).reshape(tok_rows, seq_shards * tok_rows)

    ks = (key_rows, k_x, k_p, k_d)
    vs = (value_rows, v_x, v_p, v_d)
    ctx, lse = attention_fwd(query_rows, ks, vs, mask)

    grad_context = lax.dot_general(
        cotangent, full_weight, (((1,), (1,)), ((), ())), preferred_element_type=jnp.float32
    ).astype(jnp.bfloat16)

    def reduce_parts(parts):
        back = swap(parts[2:4], "core")
        own = parts[0].astype(jnp.float32) + back[0].astype(jnp.float32)
        cross = (parts[1].astype(jnp.float32) + back[1].astype(jnp.float32)).astype(jnp.bfloat16)
        arrived = swap(cross, "y")
        return (own + arrived.astype(jnp.float32)).astype(jnp.bfloat16)

    heads = query_rows.shape[1] // HSIZE
    half = heads // 2
    pieces = []
    for first, count in ((0, half), (half, heads - half)):
        dq, dk, dv = attention_bwd(
            query_rows, ks, vs, grad_context, ctx, lse, mask, first, count
        )
        pieces.append((dq, reduce_parts(dk), reduce_parts(dv)))
    grad_queries = jnp.concatenate([p[0] for p in pieces], axis=1)
    grad_keys = jnp.concatenate([p[1] for p in pieces], axis=1)
    grad_values = jnp.concatenate([p[2] for p in pieces], axis=1)

    sublayer_out = jnp.dot(ctx, full_weight, preferred_element_type=jnp.float32).astype(
        jnp.bfloat16
    )
    return (sublayer_out, grad_queries, grad_keys, grad_values)


def solution(mesh):
    devices = mesh.devices.reshape(mesh.devices.shape[0], -1, 4, 2)
    split = Mesh(devices, ("member", "z", "y", "core"))
    rows = P(("member", "z", "y", "core"), None)
    return jax.shard_map(
        per_device,
        mesh=split,
        in_specs=(rows, rows, rows, rows, rows, P("member", None, None)),
        out_specs=(rows, rows, rows, rows),
        check_vma=False,
    )
```

```python
import functools
import math

import jax
import jax.numpy as jnp
from jax import lax
from jax.experimental import pallas as pl
from jax.experimental.pallas import tpu as pltpu
from jax.sharding import Mesh
from jax.sharding import PartitionSpec as P

HEADS = 20
HSIZE = 128
BLK = 64
QBLK = 16
NSEL = 6
LEN = 1024

SLOT_XOR = (0, 2, 1, 3)


def masked_scores(q, k, mask):
    scaling = 1.0 / math.sqrt(HSIZE)
    nt = (((1,), (1,)), ((), ()))
    s = lax.dot_general(q, k, nt, preferred_element_type=jnp.float32) * scaling
    return jnp.where(mask > 0, s, -jnp.inf)


def fwd_kernel(q_ref, k0, k1, k2, k3, v0, v1, v2, v3, mask_ref, ctx_ref, lse_ref):
    q = q_ref[...]
    k = jnp.concatenate([k0[...], k1[...], k2[...], k3[...]], axis=0)
    v = jnp.concatenate([v0[...], v1[...], v2[...], v3[...]], axis=0)
    s = masked_scores(q, k, mask_ref[...])
    m = jnp.max(s, axis=1, keepdims=True)
    e = jnp.exp(s - m)
    total = jnp.sum(e, axis=1, keepdims=True)
    lse = m + jnp.log(total)
    p_low = (e * (1.0 / total)).astype(jnp.bfloat16)
    ctx_ref[...] = jnp.dot(p_low, v, preferred_element_type=jnp.float32).astype(jnp.bfloat16)
    lse_ref[...] = lse.reshape(lse_ref.shape)


def bwd_kernel(q_ref, k0, k1, k2, k3, v0, v1, v2, v3, do_ref, ctx_ref, lse_ref, mask_ref,
               dq_ref, dk_ref, dv_ref):
    scaling = 1.0 / math.sqrt(HSIZE)
    nt = (((1,), (1,)), ((), ()))
    tn = (((0,), (0,)), ((), ()))
    q = q_ref[...]
    k = jnp.concatenate([k0[...], k1[...], k2[...], k3[...]], axis=0)
    v = jnp.concatenate([v0[...], v1[...], v2[...], v3[...]], axis=0)
    s = masked_scores(q, k, mask_ref[...])
    lse = lse_ref[...].reshape(s.shape[0], 1)
    p = jnp.exp(s - lse)
    p_low = p.astype(jnp.bfloat16)
    do = do_ref[...]
    dp = lax.dot_general(do, v, nt, preferred_element_type=jnp.float32)
    delta = jnp.sum(
        do.astype(jnp.float32) * ctx_ref[...].astype(jnp.float32), axis=1, keepdims=True
    )
    ds = (p * (dp - delta)).astype(jnp.bfloat16)
    dq = jnp.dot(ds, k, preferred_element_type=jnp.float32) * scaling
    dq_ref[...] = dq.astype(jnp.bfloat16)
    dk = lax.dot_general(ds, q, tn, preferred_element_type=jnp.float32) * scaling
    dv = lax.dot_general(p_low, do, tn, preferred_element_type=jnp.float32)
    dk_ref[...] = dk.astype(jnp.bfloat16).reshape(dk_ref.shape)
    dv_ref[...] = dv.astype(jnp.bfloat16).reshape(dv_ref.shape)


def attention_fwd(q, ks, vs, mask):
    rows, width = q.shape
    heads = width // HSIZE
    col = pl.BlockSpec((rows, HSIZE), lambda h: (0, h))
    return pl.pallas_call(
        fwd_kernel,
        grid=(heads,),
        cost_estimate=pl.CostEstimate(
            flops=heads * 2 * 10**9, transcendentals=heads * rows * 1024,
            bytes_accessed=12 * rows * width * 2,
        ),
        in_specs=[col] * 9 + [pl.BlockSpec(mask.shape, lambda h: (0, 0))],
        out_specs=[col, pl.BlockSpec((1, rows, 1), lambda h: (h, 0, 0))],
        out_shape=[
            jax.ShapeDtypeStruct((rows, width), jnp.bfloat16),
            jax.ShapeDtypeStruct((heads, rows, 1), jnp.float32),
        ],
    )(q, *ks, *vs, mask)


def attention_bwd(q, ks, vs, do, ctx, lse, mask, first, count):
    rows, width = q.shape
    col = pl.BlockSpec((rows, HSIZE), lambda h: (0, h + first))
    out_col = pl.BlockSpec((rows, HSIZE), lambda h: (0, h))
    slot_col = pl.BlockSpec((4, rows, HSIZE), lambda h: (0, 0, h))
    return pl.pallas_call(
        bwd_kernel,
        grid=(count,),
        cost_estimate=pl.CostEstimate(
            flops=count * 14 * 10**8, transcendentals=count * rows * 1024,
            bytes_accessed=12 * rows * width,
        ),
        in_specs=[col] * 11
        + [
            pl.BlockSpec((1, rows, 1), lambda h: (h + first, 0, 0)),
            pl.BlockSpec(mask.shape, lambda h: (0, 0)),
        ],
        out_specs=[out_col, slot_col, slot_col],
        out_shape=[
            jax.ShapeDtypeStruct((rows, count * HSIZE), jnp.bfloat16),
            jax.ShapeDtypeStruct((4, rows, count * HSIZE), jnp.bfloat16),
            jax.ShapeDtypeStruct((4, rows, count * HSIZE), jnp.bfloat16),
        ],
    )(q, *ks, *vs, do, ctx, lse, mask)


def swap(x, axis):
    count = lax.axis_size(axis)
    return lax.ppermute(x, axis, [(i, i ^ 1) for i in range(count)])


def per_device(query_rows, key_rows, value_rows, weight_out, cotangent, pattern):
    tok_rows = query_rows.shape[0]
    blocks_here = tok_rows // BLK
    zpos = lax.axis_index("z")
    ypos = lax.axis_index("y")
    core = lax.axis_index("core")
    seq_shards = LEN // tok_rows
    position = (ypos % 2) * 2 + core
    sequence = zpos * (lax.axis_size("y") // 2) + ypos // 2

    full_weight = lax.all_gather(weight_out, ("z", "y", "core"), axis=0, tiled=True)

    k_x = swap(key_rows, "y")
    v_x = swap(value_rows, "y")
    k_p = swap(key_rows, "core")
    v_p = swap(value_rows, "core")
    k_d = swap(k_x, "core")
    v_d = swap(v_x, "core")

    seq_plan = lax.dynamic_index_in_dim(pattern, sequence, 0, keepdims=False)
    own_plan = lax.dynamic_slice_in_dim(seq_plan, position * blocks_here, blocks_here, 0)
    rel = jnp.arange(seq_shards * tok_rows, dtype=jnp.int32) // BLK
    slot_xor = jnp.array(SLOT_XOR, dtype=jnp.int32)[rel // blocks_here]
    key_block = (position ^ slot_xor) * blocks_here + rel % blocks_here
    plan_rows = own_plan[jnp.arange(tok_rows, dtype=jnp.int32) // BLK]
    hits = [plan_rows[:, j][:, None] == key_block[None, :] for j in range(NSEL)]
    mask = functools.reduce(jnp.logical_or, hits).astype(jnp.float32)

    ks = (key_rows, k_x, k_p, k_d)
    vs = (value_rows, v_x, v_p, v_d)
    ctx, lse = attention_fwd(query_rows, ks, vs, mask)

    grad_context = lax.dot_general(
        cotangent, full_weight, (((1,), (1,)), ((), ())), preferred_element_type=jnp.float32
    ).astype(jnp.bfloat16)

    def reduce_parts(parts):
        back = swap(parts[2:4], "core")
        own = parts[0].astype(jnp.float32) + back[0].astype(jnp.float32)
        cross = (parts[1].astype(jnp.float32) + back[1].astype(jnp.float32)).astype(jnp.bfloat16)
        arrived = swap(cross, "y")
        return (own + arrived.astype(jnp.float32)).astype(jnp.bfloat16)

    heads = query_rows.shape[1] // HSIZE
    half = heads // 2
    pieces = []
    for first, count in ((0, half), (half, heads - half)):
        dq, dk, dv = attention_bwd(
            query_rows, ks, vs, grad_context, ctx, lse, mask, first, count
        )
        pieces.append((dq, reduce_parts(dk), reduce_parts(dv)))
    grad_queries = jnp.concatenate([p[0] for p in pieces], axis=1)
    grad_keys = jnp.concatenate([p[1] for p in pieces], axis=1)
    grad_values = jnp.concatenate([p[2] for p in pieces], axis=1)

    sublayer_out = jnp.dot(ctx, full_weight, preferred_element_type=jnp.float32).astype(
        jnp.bfloat16
    )
    return (sublayer_out, grad_queries, grad_keys, grad_values)


def solution(mesh):
    devices = mesh.devices.reshape(mesh.devices.shape[0], -1, 4, 2)
    split = Mesh(devices, ("member", "z", "y", "core"))
    rows = P(("member", "z", "y", "core"), None)
    return jax.shard_map(
        per_device,
        mesh=split,
        in_specs=(rows, rows, rows, rows, rows, P("member", None, None)),
        out_specs=(rows, rows, rows, rows),
        check_vma=False,
    )
```

```python
import functools
import math

import jax
import jax.numpy as jnp
from jax import lax
from jax.experimental import pallas as pl
from jax.experimental.pallas import tpu as pltpu
from jax.sharding import Mesh
from jax.sharding import PartitionSpec as P

HEADS = 20
HSIZE = 128
BLK = 64
QBLK = 16
NSEL = 6
LEN = 1024

SLOT_XOR = (0, 2, 1, 3)


def masked_scores(q, k, mask):
    scaling = 1.0 / math.sqrt(HSIZE)
    nt = (((1,), (1,)), ((), ()))
    s = lax.dot_general(q, k, nt, preferred_element_type=jnp.float32) * scaling
    return jnp.where(mask > 0, s, -jnp.inf)


def fwd_kernel(q_ref, k0, k1, k2, k3, v0, v1, v2, v3, mask_ref, ctx_ref, lse_ref):
    mask = mask_ref[...]
    for h in range(lse_ref.shape[0]):
        cols = slice(h * HSIZE, (h + 1) * HSIZE)
        q = q_ref[:, cols]
        k = jnp.concatenate([k0[:, cols], k1[:, cols], k2[:, cols], k3[:, cols]], axis=0)
        v = jnp.concatenate([v0[:, cols], v1[:, cols], v2[:, cols], v3[:, cols]], axis=0)
        s = masked_scores(q, k, mask)
        m = jnp.max(s, axis=1, keepdims=True)
        e = jnp.exp(s - m)
        total = jnp.sum(e, axis=1, keepdims=True)
        lse = m + jnp.log(total)
        p_low = (e * (1.0 / total)).astype(jnp.bfloat16)
        ctx = jnp.dot(p_low, v, preferred_element_type=jnp.float32)
        ctx_ref[:, cols] = ctx.astype(jnp.bfloat16)
        lse_ref[h] = lse


def bwd_kernel(q_ref, k0, k1, k2, k3, v0, v1, v2, v3, do_ref, ctx_ref, lse_ref, mask_ref,
               dq_ref, dk_ref, dv_ref):
    scaling = 1.0 / math.sqrt(HSIZE)
    nt = (((1,), (1,)), ((), ()))
    tn = (((0,), (0,)), ((), ()))
    mask = mask_ref[...]
    for h in range(lse_ref.shape[0]):
        cols = slice(h * HSIZE, (h + 1) * HSIZE)
        q = q_ref[:, cols]
        k = jnp.concatenate([k0[:, cols], k1[:, cols], k2[:, cols], k3[:, cols]], axis=0)
        v = jnp.concatenate([v0[:, cols], v1[:, cols], v2[:, cols], v3[:, cols]], axis=0)
        s = masked_scores(q, k, mask)
        p = jnp.exp(s - lse_ref[h])
        p_low = p.astype(jnp.bfloat16)
        do = do_ref[:, cols]
        dp = lax.dot_general(do, v, nt, preferred_element_type=jnp.float32)
        delta = jnp.sum(
            do.astype(jnp.float32) * ctx_ref[:, cols].astype(jnp.float32), axis=1, keepdims=True
        )
        ds = (p * (dp - delta)).astype(jnp.bfloat16)
        dq = jnp.dot(ds, k, preferred_element_type=jnp.float32) * scaling
        dq_ref[:, cols] = dq.astype(jnp.bfloat16)
        dk = lax.dot_general(ds, q, tn, preferred_element_type=jnp.float32) * scaling
        dv = lax.dot_general(p_low, do, tn, preferred_element_type=jnp.float32)
        dk_ref[:, :, cols] = dk.astype(jnp.bfloat16).reshape(4, -1, HSIZE)
        dv_ref[:, :, cols] = dv.astype(jnp.bfloat16).reshape(4, -1, HSIZE)


def attention_fwd(q, ks, vs, mask, per_step):
    rows, width = q.shape
    heads = width // HSIZE
    col = pl.BlockSpec((rows, per_step * HSIZE), lambda h: (0, h))
    return pl.pallas_call(
        fwd_kernel,
        grid=(heads // per_step,),
        cost_estimate=pl.CostEstimate(
            flops=heads * 2 * 10**9, transcendentals=heads * rows * 1024,
            bytes_accessed=12 * rows * width * 2,
        ),
        in_specs=[col] * 9 + [pl.BlockSpec(mask.shape, lambda h: (0, 0))],
        out_specs=[col, pl.BlockSpec((per_step, rows, 1), lambda h: (h, 0, 0))],
        out_shape=[
            jax.ShapeDtypeStruct((rows, width), jnp.bfloat16),
            jax.ShapeDtypeStruct((heads, rows, 1), jnp.float32),
        ],
    )(q, *ks, *vs, mask)


def attention_bwd(q, ks, vs, do, ctx, lse, mask, first, count, per_step):
    rows, width = q.shape
    lead = first // per_step
    span = per_step * HSIZE
    col = pl.BlockSpec((rows, span), lambda h: (0, h + lead))
    out_col = pl.BlockSpec((rows, span), lambda h: (0, h))
    slot_col = pl.BlockSpec((4, rows, span), lambda h: (0, 0, h))
    return pl.pallas_call(
        bwd_kernel,
        grid=(count // per_step,),
        cost_estimate=pl.CostEstimate(
            flops=count * 14 * 10**8, transcendentals=count * rows * 1024,
            bytes_accessed=12 * rows * width,
        ),
        in_specs=[col] * 11
        + [
            pl.BlockSpec((per_step, rows, 1), lambda h: (h + lead, 0, 0)),
            pl.BlockSpec(mask.shape, lambda h: (0, 0)),
        ],
        out_specs=[out_col, slot_col, slot_col],
        out_shape=[
            jax.ShapeDtypeStruct((rows, count * HSIZE), jnp.bfloat16),
            jax.ShapeDtypeStruct((4, rows, count * HSIZE), jnp.bfloat16),
            jax.ShapeDtypeStruct((4, rows, count * HSIZE), jnp.bfloat16),
        ],
    )(q, *ks, *vs, do, ctx, lse, mask)


def swap(x, axis):
    count = lax.axis_size(axis)
    return lax.ppermute(x, axis, [(i, i ^ 1) for i in range(count)])


def per_device(query_rows, key_rows, value_rows, weight_out, cotangent, pattern):
    tok_rows = query_rows.shape[0]
    blocks_here = tok_rows // BLK
    zpos = lax.axis_index("z")
    ypos = lax.axis_index("y")
    core = lax.axis_index("core")
    seq_shards = LEN // tok_rows
    position = (ypos % 2) * 2 + core
    sequence = zpos * (lax.axis_size("y") // 2) + ypos // 2

    full_weight = lax.all_gather(weight_out, ("z", "y", "core"), axis=0, tiled=True)

    k_x = swap(key_rows, "y")
    v_x = swap(value_rows, "y")
    k_p = swap(key_rows, "core")
    v_p = swap(value_rows, "core")
    k_d = swap(k_x, "core")
    v_d = swap(v_x, "core")

    seq_plan = lax.dynamic_index_in_dim(pattern, sequence, 0, keepdims=False)
    own_plan = lax.dynamic_slice_in_dim(seq_plan, position * blocks_here, blocks_here, 0)
    rel = jnp.arange(seq_shards * tok_rows, dtype=jnp.int32) // BLK
    slot_xor = jnp.array(SLOT_XOR, dtype=jnp.int32)[rel // blocks_here]
    key_block = (position ^ slot_xor) * blocks_here + rel % blocks_here
    plan_rows = own_plan[jnp.arange(tok_rows, dtype=jnp.int32) // BLK]
    hits = [plan_rows[:, j][:, None] == key_block[None, :] for j in range(NSEL)]
    mask = functools.reduce(jnp.logical_or, hits).astype(jnp.float32)

    ks = (key_rows, k_x, k_p, k_d)
    vs = (value_rows, v_x, v_p, v_d)
    ctx, lse = attention_fwd(query_rows, ks, vs, mask, 4)

    grad_context = lax.dot_general(
        cotangent, full_weight, (((1,), (1,)), ((), ())), preferred_element_type=jnp.float32
    ).astype(jnp.bfloat16)

    def presum(parts):
        back = swap(parts[2:4], "core")
        own = parts[0].astype(jnp.float32) + back[0].astype(jnp.float32)
        cross = (parts[1].astype(jnp.float32) + back[1].astype(jnp.float32)).astype(jnp.bfloat16)
        return own, cross

    def finish(own, cross):
        arrived = swap(cross, "y")
        return (own + arrived.astype(jnp.float32)).astype(jnp.bfloat16)

    heads = query_rows.shape[1] // HSIZE
    half = heads // 2
    pieces = []
    later = (query_rows, grad_context, ctx)
    for first, count in ((0, half), (half, heads - half)):
        q_in, do_in, ctx_in = later
        dq, dk, dv = attention_bwd(q_in, ks, vs, do_in, ctx_in, lse, mask, first, count, 2)
        k_own, k_cross = presum(dk)
        v_own, v_cross = presum(dv)
        later, k_cross, v_cross = lax.optimization_barrier((later, k_cross, v_cross))
        pieces.append((dq, finish(k_own, k_cross), finish(v_own, v_cross)))
    grad_queries = jnp.concatenate([p[0] for p in pieces], axis=1)
    grad_keys = jnp.concatenate([p[1] for p in pieces], axis=1)
    grad_values = jnp.concatenate([p[2] for p in pieces], axis=1)

    ctx_out = later[2]
    sublayer_out = jnp.dot(ctx_out, full_weight, preferred_element_type=jnp.float32).astype(
        jnp.bfloat16
    )
    return (sublayer_out, grad_queries, grad_keys, grad_values)


def solution(mesh):
    devices = mesh.devices.reshape(mesh.devices.shape[0], -1, 4, 2)
    split = Mesh(devices, ("member", "z", "y", "core"))
    rows = P(("member", "z", "y", "core"), None)
    return jax.shard_map(
        per_device,
        mesh=split,
        in_specs=(rows, rows, rows, rows, rows, P("member", None, None)),
        out_specs=(rows, rows, rows, rows),
        check_vma=False,
    )
```

```python
import functools
import math

import jax
import jax.numpy as jnp
from jax import lax
from jax.experimental import pallas as pl
from jax.experimental.pallas import tpu as pltpu
from jax.sharding import Mesh
from jax.sharding import PartitionSpec as P

HEADS = 20
HSIZE = 128
BLK = 64
QBLK = 16
NSEL = 6
LEN = 1024

SLOT_XOR = (0, 2, 1, 3)


def masked_scores(q, k, mask):
    scaling = 1.0 / math.sqrt(HSIZE)
    nt = (((1,), (1,)), ((), ()))
    s = lax.dot_general(q, k, nt, preferred_element_type=jnp.float32) * scaling
    return jnp.where(mask > 0, s, -jnp.inf)


def fwd_kernel(q_ref, k0, k1, k2, k3, v0, v1, v2, v3, mask_ref, ctx_ref, lse_ref):
    mask = mask_ref[...]
    for h in range(lse_ref.shape[0]):
        cols = slice(h * HSIZE, (h + 1) * HSIZE)
        q = q_ref[:, cols]
        k = jnp.concatenate([k0[:, cols], k1[:, cols], k2[:, cols], k3[:, cols]], axis=0)
        v = jnp.concatenate([v0[:, cols], v1[:, cols], v2[:, cols], v3[:, cols]], axis=0)
        s = masked_scores(q, k, mask)
        m = jnp.max(s, axis=1, keepdims=True)
        e = jnp.exp(s - m)
        total = jnp.sum(e, axis=1, keepdims=True)
        lse = m + jnp.log(total)
        p_low = (e * (1.0 / total)).astype(jnp.bfloat16)
        ctx = jnp.dot(p_low, v, preferred_element_type=jnp.float32)
        ctx_ref[:, cols] = ctx.astype(jnp.bfloat16)
        lse_ref[h] = lse


def bwd_kernel(q_ref, k0, k1, k2, k3, v0, v1, v2, v3, do_ref, ctx_ref, lse_ref, mask_ref,
               dq_ref, dkv_ref):
    scaling = 1.0 / math.sqrt(HSIZE)
    nt = (((1,), (1,)), ((), ()))
    tn = (((0,), (0,)), ((), ()))
    mask = mask_ref[...]
    for h in range(lse_ref.shape[0]):
        cols = slice(h * HSIZE, (h + 1) * HSIZE)
        q = q_ref[:, cols]
        k = jnp.concatenate([k0[:, cols], k1[:, cols], k2[:, cols], k3[:, cols]], axis=0)
        v = jnp.concatenate([v0[:, cols], v1[:, cols], v2[:, cols], v3[:, cols]], axis=0)
        s = masked_scores(q, k, mask)
        p = jnp.exp(s - lse_ref[h])
        p_low = p.astype(jnp.bfloat16)
        do = do_ref[:, cols]
        dp = lax.dot_general(do, v, nt, preferred_element_type=jnp.float32)
        delta = jnp.sum(
            do.astype(jnp.float32) * ctx_ref[:, cols].astype(jnp.float32), axis=1, keepdims=True
        )
        ds = (p * (dp - delta)).astype(jnp.bfloat16)
        dq = jnp.dot(ds, k, preferred_element_type=jnp.float32) * scaling
        dq_ref[:, cols] = dq.astype(jnp.bfloat16)
        dk = lax.dot_general(ds, q, tn, preferred_element_type=jnp.float32) * scaling
        dv = lax.dot_general(p_low, do, tn, preferred_element_type=jnp.float32)
        dkv_ref[:, 0, :, cols] = dk.astype(jnp.bfloat16).reshape(4, -1, HSIZE)
        dkv_ref[:, 1, :, cols] = dv.astype(jnp.bfloat16).reshape(4, -1, HSIZE)


def attention_fwd(q, ks, vs, mask, per_step):
    rows, width = q.shape
    heads = width // HSIZE
    col = pl.BlockSpec((rows, per_step * HSIZE), lambda h: (0, h))
    return pl.pallas_call(
        fwd_kernel,
        grid=(heads // per_step,),
        cost_estimate=pl.CostEstimate(
            flops=heads * 2 * 10**9, transcendentals=heads * rows * 1024,
            bytes_accessed=12 * rows * width * 2,
        ),
        in_specs=[col] * 9 + [pl.BlockSpec(mask.shape, lambda h: (0, 0))],
        out_specs=[col, pl.BlockSpec((per_step, rows, 1), lambda h: (h, 0, 0))],
        out_shape=[
            jax.ShapeDtypeStruct((rows, width), jnp.bfloat16),
            jax.ShapeDtypeStruct((heads, rows, 1), jnp.float32),
        ],
    )(q, *ks, *vs, mask)


def attention_bwd(q, ks, vs, do, ctx, lse, mask, first, count, per_step):
    rows, width = q.shape
    lead = first // per_step
    span = per_step * HSIZE
    col = pl.BlockSpec((rows, span), lambda h: (0, h + lead))
    out_col = pl.BlockSpec((rows, span), lambda h: (0, h))
    slot_col = pl.BlockSpec((4, 2, rows, span), lambda h: (0, 0, 0, h))
    return pl.pallas_call(
        bwd_kernel,
        grid=(count // per_step,),
        cost_estimate=pl.CostEstimate(
            flops=count * 14 * 10**8, transcendentals=count * rows * 1024,
            bytes_accessed=12 * rows * width,
        ),
        in_specs=[col] * 11
        + [
            pl.BlockSpec((per_step, rows, 1), lambda h: (h + lead, 0, 0)),
            pl.BlockSpec(mask.shape, lambda h: (0, 0)),
        ],
        out_specs=[out_col, slot_col],
        out_shape=[
            jax.ShapeDtypeStruct((rows, count * HSIZE), jnp.bfloat16),
            jax.ShapeDtypeStruct((4, 2, rows, count * HSIZE), jnp.bfloat16),
        ],
    )(q, *ks, *vs, do, ctx, lse, mask)


def swap(x, axis):
    count = lax.axis_size(axis)
    return lax.ppermute(x, axis, [(i, i ^ 1) for i in range(count)])


def per_device(query_rows, key_rows, value_rows, weight_out, cotangent, pattern):
    tok_rows = query_rows.shape[0]
    blocks_here = tok_rows // BLK
    zpos = lax.axis_index("z")
    ypos = lax.axis_index("y")
    core = lax.axis_index("core")
    seq_shards = LEN // tok_rows
    position = (ypos % 2) * 2 + core
    sequence = zpos * (lax.axis_size("y") // 2) + ypos // 2

    full_weight = lax.all_gather(weight_out, ("z", "y", "core"), axis=0, tiled=True)

    k_x = swap(key_rows, "y")
    v_x = swap(value_rows, "y")
    k_p = swap(key_rows, "core")
    v_p = swap(value_rows, "core")
    k_d = swap(k_x, "core")
    v_d = swap(v_x, "core")

    seq_plan = lax.dynamic_index_in_dim(pattern, sequence, 0, keepdims=False)
    own_plan = lax.dynamic_slice_in_dim(seq_plan, position * blocks_here, blocks_here, 0)
    rel = jnp.arange(seq_shards * tok_rows, dtype=jnp.int32) // BLK
    slot_xor = jnp.array(SLOT_XOR, dtype=jnp.int32)[rel // blocks_here]
    key_block = (position ^ slot_xor) * blocks_here + rel % blocks_here
    plan_rows = own_plan[jnp.arange(tok_rows, dtype=jnp.int32) // BLK]
    hits = [plan_rows[:, j][:, None] == key_block[None, :] for j in range(NSEL)]
    mask = functools.reduce(jnp.logical_or, hits).astype(jnp.float32)

    ks = (key_rows, k_x, k_p, k_d)
    vs = (value_rows, v_x, v_p, v_d)
    ctx, lse = attention_fwd(query_rows, ks, vs, mask, 4)

    grad_context = lax.dot_general(
        cotangent, full_weight, (((1,), (1,)), ((), ())), preferred_element_type=jnp.float32
    ).astype(jnp.bfloat16)

    def presum(parts):
        back = swap(parts[2:4], "core")
        own = parts[0].astype(jnp.float32) + back[0].astype(jnp.float32)
        cross = (parts[1].astype(jnp.float32) + back[1].astype(jnp.float32)).astype(jnp.bfloat16)
        return own, cross

    def finish(own, cross):
        arrived = swap(cross, "y")
        return (own + arrived.astype(jnp.float32)).astype(jnp.bfloat16)

    heads = query_rows.shape[1] // HSIZE
    half = heads // 2
    later = (query_rows, grad_context, ctx)
    q_in, do_in, ctx_in = later
    dq_a, dkv_a = attention_bwd(q_in, ks, vs, do_in, ctx_in, lse, mask, 0, half, 2)
    own_a, cross_a = presum(dkv_a)
    later, cross_a = lax.optimization_barrier((later, cross_a))
    arrived_a = swap(cross_a, "y")
    q_in, do_in, ctx_in = later
    dq_b, dkv_b = attention_bwd(q_in, ks, vs, do_in, ctx_in, lse, mask, half, heads - half, 2)
    dkv_b, arrived_a = lax.optimization_barrier((dkv_b, arrived_a))
    res_a = (own_a + arrived_a.astype(jnp.float32)).astype(jnp.bfloat16)
    own_b, cross_b = presum(dkv_b)
    later, cross_b = lax.optimization_barrier((later, cross_b))
    res_b = finish(own_b, cross_b)
    grad_queries = jnp.concatenate([dq_a, dq_b], axis=1)
    grad_keys = jnp.concatenate([res_a[0], res_b[0]], axis=1)
    grad_values = jnp.concatenate([res_a[1], res_b[1]], axis=1)

    ctx_out = later[2]
    sublayer_out = jnp.dot(ctx_out, full_weight, preferred_element_type=jnp.float32).astype(
        jnp.bfloat16
    )
    return (sublayer_out, grad_queries, grad_keys, grad_values)


def solution(mesh):
    devices = mesh.devices.reshape(mesh.devices.shape[0], -1, 4, 2)
    split = Mesh(devices, ("member", "z", "y", "core"))
    rows = P(("member", "z", "y", "core"), None)
    return jax.shard_map(
        per_device,
        mesh=split,
        in_specs=(rows, rows, rows, rows, rows, P("member", None, None)),
        out_specs=(rows, rows, rows, rows),
        check_vma=False,
    )
```

```python
import functools
import math

import jax
import jax.numpy as jnp
from jax import lax
from jax.experimental import pallas as pl
from jax.experimental.pallas import tpu as pltpu
from jax.sharding import Mesh
from jax.sharding import PartitionSpec as P

HEADS = 20
HSIZE = 128
BLK = 64
QBLK = 16
NSEL = 6
LEN = 1024

SLOT_XOR = (0, 2, 1, 3)


def masked_scores(q, k, mask):
    scaling = 1.0 / math.sqrt(HSIZE)
    nt = (((1,), (1,)), ((), ()))
    s = lax.dot_general(q, k, nt, preferred_element_type=jnp.float32) * scaling
    return jnp.where(mask > 0, s, -jnp.inf)


def fwd_kernel(q_ref, k0, k1, k2, k3, v0, v1, v2, v3, mask_ref, ctx_ref, lse_ref):
    mask = mask_ref[...]
    for h in range(lse_ref.shape[0]):
        cols = slice(h * HSIZE, (h + 1) * HSIZE)
        q = q_ref[:, cols]
        k = jnp.concatenate([k0[:, cols], k1[:, cols], k2[:, cols], k3[:, cols]], axis=0)
        v = jnp.concatenate([v0[:, cols], v1[:, cols], v2[:, cols], v3[:, cols]], axis=0)
        s = masked_scores(q, k, mask)
        m = jnp.max(s, axis=1, keepdims=True)
        e = jnp.exp(s - m)
        total = jnp.sum(e, axis=1, keepdims=True)
        lse = m + jnp.log(total)
        p_low = (e * (1.0 / total)).astype(jnp.bfloat16)
        ctx = jnp.dot(p_low, v, preferred_element_type=jnp.float32)
        ctx_ref[:, cols] = ctx.astype(jnp.bfloat16)
        lse_ref[h] = lse


def bwd_kernel(q_ref, k0, k1, k2, k3, v0, v1, v2, v3, do_ref, ctx_ref, lse_ref, mask_ref,
               dq_ref, dk_ref, dv_ref):
    scaling = 1.0 / math.sqrt(HSIZE)
    nt = (((1,), (1,)), ((), ()))
    tn = (((0,), (0,)), ((), ()))
    mask = mask_ref[...]
    for h in range(lse_ref.shape[0]):
        cols = slice(h * HSIZE, (h + 1) * HSIZE)
        q = q_ref[:, cols]
        k = jnp.concatenate([k0[:, cols], k1[:, cols], k2[:, cols], k3[:, cols]], axis=0)
        v = jnp.concatenate([v0[:, cols], v1[:, cols], v2[:, cols], v3[:, cols]], axis=0)
        s = masked_scores(q, k, mask)
        p = jnp.exp(s - lse_ref[h])
        p_low = p.astype(jnp.bfloat16)
        do = do_ref[:, cols]
        dp = lax.dot_general(do, v, nt, preferred_element_type=jnp.float32)
        delta = jnp.sum(
            do.astype(jnp.float32) * ctx_ref[:, cols].astype(jnp.float32), axis=1, keepdims=True
        )
        ds = (p * (dp - delta)).astype(jnp.bfloat16)
        dq = jnp.dot(ds, k, preferred_element_type=jnp.float32) * scaling
        dq_ref[:, cols] = dq.astype(jnp.bfloat16)
        dk = lax.dot_general(ds, q, tn, preferred_element_type=jnp.float32) * scaling
        dv = lax.dot_general(p_low, do, tn, preferred_element_type=jnp.float32)
        dk_ref[:, :, cols] = dk.astype(jnp.bfloat16).reshape(4, -1, HSIZE)
        dv_ref[:, :, cols] = dv.astype(jnp.bfloat16).reshape(4, -1, HSIZE)


def attention_fwd(q, ks, vs, mask, per_step):
    rows, width = q.shape
    heads = width // HSIZE
    col = pl.BlockSpec((rows, per_step * HSIZE), lambda h: (0, h))
    return pl.pallas_call(
        fwd_kernel,
        grid=(heads // per_step,),
        cost_estimate=pl.CostEstimate(
            flops=heads * 2 * 10**9, transcendentals=heads * rows * 1024,
            bytes_accessed=12 * rows * width * 2,
        ),
        in_specs=[col] * 9 + [pl.BlockSpec(mask.shape, lambda h: (0, 0))],
        out_specs=[col, pl.BlockSpec((per_step, rows, 1), lambda h: (h, 0, 0))],
        out_shape=[
            jax.ShapeDtypeStruct((rows, width), jnp.bfloat16),
            jax.ShapeDtypeStruct((heads, rows, 1), jnp.float32),
        ],
    )(q, *ks, *vs, mask)


def attention_bwd(q, ks, vs, do, ctx, lse, mask, first, count, per_step):
    rows, width = q.shape
    lead = first // per_step
    span = per_step * HSIZE
    col = pl.BlockSpec((rows, span), lambda h: (0, h + lead))
    out_col = pl.BlockSpec((rows, span), lambda h: (0, h))
    slot_col = pl.BlockSpec((4, rows, span), lambda h: (0, 0, h))
    return pl.pallas_call(
        bwd_kernel,
        grid=(count // per_step,),
        cost_estimate=pl.CostEstimate(
            flops=count * 14 * 10**8, transcendentals=count * rows * 1024,
            bytes_accessed=12 * rows * width,
        ),
        in_specs=[col] * 9
        + [out_col, col]
        + [
            pl.BlockSpec((per_step, rows, 1), lambda h: (h + lead, 0, 0)),
            pl.BlockSpec(mask.shape, lambda h: (0, 0)),
        ],
        out_specs=[out_col, slot_col, slot_col],
        out_shape=[
            jax.ShapeDtypeStruct((rows, count * HSIZE), jnp.bfloat16),
            jax.ShapeDtypeStruct((4, rows, count * HSIZE), jnp.bfloat16),
            jax.ShapeDtypeStruct((4, rows, count * HSIZE), jnp.bfloat16),
        ],
    )(q, *ks, *vs, do, ctx, lse, mask)


def swap(x, axis):
    count = lax.axis_size(axis)
    return lax.ppermute(x, axis, [(i, i ^ 1) for i in range(count)])


def per_device(query_rows, key_rows, value_rows, weight_out, cotangent, pattern):
    tok_rows = query_rows.shape[0]
    blocks_here = tok_rows // BLK
    zpos = lax.axis_index("z")
    ypos = lax.axis_index("y")
    core = lax.axis_index("core")
    seq_shards = LEN // tok_rows
    position = (ypos % 2) * 2 + core
    sequence = zpos * (lax.axis_size("y") // 2) + ypos // 2

    full_weight = lax.all_gather(weight_out, ("z", "y", "core"), axis=0, tiled=True)

    k_x = swap(key_rows, "y")
    v_x = swap(value_rows, "y")
    k_p = swap(key_rows, "core")
    v_p = swap(value_rows, "core")
    k_d = swap(k_x, "core")
    v_d = swap(v_x, "core")

    seq_plan = lax.dynamic_index_in_dim(pattern, sequence, 0, keepdims=False)
    own_plan = lax.dynamic_slice_in_dim(seq_plan, position * blocks_here, blocks_here, 0)
    rel = jnp.arange(seq_shards * tok_rows, dtype=jnp.int32) // BLK
    slot_xor = jnp.array(SLOT_XOR, dtype=jnp.int32)[rel // blocks_here]
    key_block = (position ^ slot_xor) * blocks_here + rel % blocks_here
    plan_rows = own_plan[jnp.arange(tok_rows, dtype=jnp.int32) // BLK]
    hits = [plan_rows[:, j][:, None] == key_block[None, :] for j in range(NSEL)]
    mask = functools.reduce(jnp.logical_or, hits).astype(jnp.float32)

    ks = (key_rows, k_x, k_p, k_d)
    vs = (value_rows, v_x, v_p, v_d)
    ctx, lse = attention_fwd(query_rows, ks, vs, mask, 4)


    def presum(parts):
        back = swap(parts[2:4], "core")
        own = parts[0].astype(jnp.float32) + back[0].astype(jnp.float32)
        cross = (parts[1].astype(jnp.float32) + back[1].astype(jnp.float32)).astype(jnp.bfloat16)
        return own, cross

    def finish(own, cross):
        arrived = swap(cross, "y")
        return (own + arrived.astype(jnp.float32)).astype(jnp.bfloat16)

    heads = query_rows.shape[1] // HSIZE
    half = heads // 2
    pieces = []
    later = (query_rows, ctx)
    for first, count in ((0, half), (half, heads - half)):
        q_in, ctx_in = later
        w_rows = lax.slice_in_dim(full_weight, first * HSIZE, (first + count) * HSIZE, axis=0)
        do_part = lax.dot_general(
            cotangent, w_rows, (((1,), (1,)), ((), ())), preferred_element_type=jnp.float32
        ).astype(jnp.bfloat16)
        dq, dk, dv = attention_bwd(q_in, ks, vs, do_part, ctx_in, lse, mask, first, count, 2)
        k_own, k_cross = presum(dk)
        v_own, v_cross = presum(dv)
        later, k_cross, v_cross = lax.optimization_barrier((later, k_cross, v_cross))
        pieces.append((dq, finish(k_own, k_cross), finish(v_own, v_cross)))
    grad_queries = jnp.concatenate([p[0] for p in pieces], axis=1)
    grad_keys = jnp.concatenate([p[1] for p in pieces], axis=1)
    grad_values = jnp.concatenate([p[2] for p in pieces], axis=1)

    ctx_out = later[1]
    sublayer_out = jnp.dot(ctx_out, full_weight, preferred_element_type=jnp.float32).astype(
        jnp.bfloat16
    )
    return (sublayer_out, grad_queries, grad_keys, grad_values)


def solution(mesh):
    devices = mesh.devices.reshape(mesh.devices.shape[0], -1, 4, 2)
    split = Mesh(devices, ("member", "z", "y", "core"))
    rows = P(("member", "z", "y", "core"), None)
    return jax.shard_map(
        per_device,
        mesh=split,
        in_specs=(rows, rows, rows, rows, rows, P("member", None, None)),
        out_specs=(rows, rows, rows, rows),
        check_vma=False,
    )
```

```python
import functools
import math

import jax
import jax.numpy as jnp
from jax import lax
from jax.experimental import pallas as pl
from jax.experimental.pallas import tpu as pltpu
from jax.sharding import Mesh
from jax.sharding import PartitionSpec as P

HEADS = 20
HSIZE = 128
BLK = 64
QBLK = 16
NSEL = 6
LEN = 1024

SLOT_XOR = (0, 2, 1, 3)


def masked_scores(q, k, mask):
    scaling = 1.0 / math.sqrt(HSIZE)
    nt = (((1,), (1,)), ((), ()))
    s = lax.dot_general(q, k, nt, preferred_element_type=jnp.float32) * scaling
    return jnp.where(mask > 0, s, -jnp.inf)


def fwd_kernel(q_ref, k0, k1, k2, k3, v0, v1, v2, v3, mask_ref, ctx_ref, lse_ref):
    mask = mask_ref[...]
    for h in range(lse_ref.shape[0]):
        cols = slice(h * HSIZE, (h + 1) * HSIZE)
        q = q_ref[:, cols]
        k = jnp.concatenate([k0[:, cols], k1[:, cols], k2[:, cols], k3[:, cols]], axis=0)
        v = jnp.concatenate([v0[:, cols], v1[:, cols], v2[:, cols], v3[:, cols]], axis=0)
        s = masked_scores(q, k, mask)
        m = jnp.max(s, axis=1, keepdims=True)
        e = jnp.exp(s - m)
        total = jnp.sum(e, axis=1, keepdims=True)
        lse = m + jnp.log(total)
        p_low = (e * (1.0 / total)).astype(jnp.bfloat16)
        ctx = jnp.dot(p_low, v, preferred_element_type=jnp.float32)
        ctx_ref[:, cols] = ctx.astype(jnp.bfloat16)
        lse_ref[h] = lse


def bwd_kernel(q_ref, k0, k1, k2, k3, v0, v1, v2, v3, do_ref, ctx_ref, lse_ref, mask_ref,
               dq_ref, dk_keep, dk_send, dv_keep, dv_send):
    scaling = 1.0 / math.sqrt(HSIZE)
    nt = (((1,), (1,)), ((), ()))
    tn = (((0,), (0,)), ((), ()))
    mask = mask_ref[...]
    for h in range(lse_ref.shape[0]):
        cols = slice(h * HSIZE, (h + 1) * HSIZE)
        q = q_ref[:, cols]
        k = jnp.concatenate([k0[:, cols], k1[:, cols], k2[:, cols], k3[:, cols]], axis=0)
        v = jnp.concatenate([v0[:, cols], v1[:, cols], v2[:, cols], v3[:, cols]], axis=0)
        s = masked_scores(q, k, mask)
        p = jnp.exp(s - lse_ref[h])
        p_low = p.astype(jnp.bfloat16)
        do = do_ref[:, cols]
        dp = lax.dot_general(do, v, nt, preferred_element_type=jnp.float32)
        delta = jnp.sum(
            do.astype(jnp.float32) * ctx_ref[:, cols].astype(jnp.float32), axis=1, keepdims=True
        )
        ds = (p * (dp - delta)).astype(jnp.bfloat16)
        dq = jnp.dot(ds, k, preferred_element_type=jnp.float32) * scaling
        dq_ref[:, cols] = dq.astype(jnp.bfloat16)
        dk = lax.dot_general(ds, q, tn, preferred_element_type=jnp.float32) * scaling
        dv = lax.dot_general(p_low, do, tn, preferred_element_type=jnp.float32)
        dk = dk.astype(jnp.bfloat16).reshape(4, -1, HSIZE)
        dv = dv.astype(jnp.bfloat16).reshape(4, -1, HSIZE)
        dk_keep[:, :, cols] = dk[0:2]
        dk_send[:, :, cols] = dk[2:4]
        dv_keep[:, :, cols] = dv[0:2]
        dv_send[:, :, cols] = dv[2:4]


def attention_fwd(q, ks, vs, mask, per_step):
    rows, width = q.shape
    heads = width // HSIZE
    col = pl.BlockSpec((rows, per_step * HSIZE), lambda h: (0, h))
    return pl.pallas_call(
        fwd_kernel,
        grid=(heads // per_step,),
        cost_estimate=pl.CostEstimate(
            flops=heads * 2 * 10**9, transcendentals=heads * rows * 1024,
            bytes_accessed=12 * rows * width * 2,
        ),
        in_specs=[col] * 9 + [pl.BlockSpec(mask.shape, lambda h: (0, 0))],
        out_specs=[col, pl.BlockSpec((per_step, rows, 1), lambda h: (h, 0, 0))],
        out_shape=[
            jax.ShapeDtypeStruct((rows, width), jnp.bfloat16),
            jax.ShapeDtypeStruct((heads, rows, 1), jnp.float32),
        ],
    )(q, *ks, *vs, mask)


def attention_bwd(q, ks, vs, do, ctx, lse, mask, first, count, per_step):
    rows, width = q.shape
    lead = first // per_step
    span = per_step * HSIZE
    col = pl.BlockSpec((rows, span), lambda h: (0, h + lead))
    out_col = pl.BlockSpec((rows, span), lambda h: (0, h))
    slot_col = pl.BlockSpec((2, rows, span), lambda h: (0, 0, h))
    return pl.pallas_call(
        bwd_kernel,
        grid=(count // per_step,),
        cost_estimate=pl.CostEstimate(
            flops=count * 14 * 10**8, transcendentals=count * rows * 1024,
            bytes_accessed=12 * rows * width,
        ),
        in_specs=[col] * 9
        + [out_col, col]
        + [
            pl.BlockSpec((per_step, rows, 1), lambda h: (h + lead, 0, 0)),
            pl.BlockSpec(mask.shape, lambda h: (0, 0)),
        ],
        out_specs=[out_col] + [slot_col] * 4,
        out_shape=[jax.ShapeDtypeStruct((rows, count * HSIZE), jnp.bfloat16)]
        + [jax.ShapeDtypeStruct((2, rows, count * HSIZE), jnp.bfloat16)] * 4,
    )(q, *ks, *vs, do, ctx, lse, mask)


def swap(x, axis):
    count = lax.axis_size(axis)
    return lax.ppermute(x, axis, [(i, i ^ 1) for i in range(count)])


def per_device(query_rows, key_rows, value_rows, weight_out, cotangent, pattern):
    tok_rows = query_rows.shape[0]
    blocks_here = tok_rows // BLK
    zpos = lax.axis_index("z")
    ypos = lax.axis_index("y")
    core = lax.axis_index("core")
    seq_shards = LEN // tok_rows
    position = (ypos % 2) * 2 + core
    sequence = zpos * (lax.axis_size("y") // 2) + ypos // 2

    full_weight = lax.all_gather(weight_out, ("z", "y", "core"), axis=0, tiled=True)

    k_x = swap(key_rows, "y")
    v_x = swap(value_rows, "y")
    k_p = swap(key_rows, "core")
    v_p = swap(value_rows, "core")
    k_d = swap(k_x, "core")
    v_d = swap(v_x, "core")

    seq_plan = lax.dynamic_index_in_dim(pattern, sequence, 0, keepdims=False)
    own_plan = lax.dynamic_slice_in_dim(seq_plan, position * blocks_here, blocks_here, 0)
    rel = jnp.arange(seq_shards * tok_rows, dtype=jnp.int32) // BLK
    slot_xor = jnp.array(SLOT_XOR, dtype=jnp.int32)[rel // blocks_here]
    key_block = (position ^ slot_xor) * blocks_here + rel % blocks_here
    plan_rows = own_plan[jnp.arange(tok_rows, dtype=jnp.int32) // BLK]
    hits = [plan_rows[:, j][:, None] == key_block[None, :] for j in range(NSEL)]
    mask = functools.reduce(jnp.logical_or, hits).astype(jnp.float32)

    ks = (key_rows, k_x, k_p, k_d)
    vs = (value_rows, v_x, v_p, v_d)
    ctx, lse = attention_fwd(query_rows, ks, vs, mask, 4)


    def presum(keep, send):
        back = swap(send, "core")
        own = keep[0].astype(jnp.float32) + back[0].astype(jnp.float32)
        cross = (keep[1].astype(jnp.float32) + back[1].astype(jnp.float32)).astype(jnp.bfloat16)
        return own, cross

    def finish(own, cross):
        arrived = swap(cross, "y")
        return (own + arrived.astype(jnp.float32)).astype(jnp.bfloat16)

    heads = query_rows.shape[1] // HSIZE
    half = heads // 2
    pieces = []
    later = (query_rows, ctx)
    for first, count in ((0, half), (half, heads - half)):
        q_in, ctx_in = later
        w_rows = lax.slice_in_dim(full_weight, first * HSIZE, (first + count) * HSIZE, axis=0)
        do_part = lax.dot_general(
            cotangent, w_rows, (((1,), (1,)), ((), ())), preferred_element_type=jnp.float32
        ).astype(jnp.bfloat16)
        dq, dk_keep, dk_send, dv_keep, dv_send = attention_bwd(
            q_in, ks, vs, do_part, ctx_in, lse, mask, first, count, 2
        )
        k_own, k_cross = presum(dk_keep, dk_send)
        v_own, v_cross = presum(dv_keep, dv_send)
        later, k_cross, v_cross = lax.optimization_barrier((later, k_cross, v_cross))
        pieces.append((dq, finish(k_own, k_cross), finish(v_own, v_cross)))
    grad_queries = jnp.concatenate([p[0] for p in pieces], axis=1)
    grad_keys = jnp.concatenate([p[1] for p in pieces], axis=1)
    grad_values = jnp.concatenate([p[2] for p in pieces], axis=1)

    ctx_out = later[1]
    sublayer_out = jnp.dot(ctx_out, full_weight, preferred_element_type=jnp.float32).astype(
        jnp.bfloat16
    )
    return (sublayer_out, grad_queries, grad_keys, grad_values)


def solution(mesh):
    devices = mesh.devices.reshape(mesh.devices.shape[0], -1, 4, 2)
    split = Mesh(devices, ("member", "z", "y", "core"))
    rows = P(("member", "z", "y", "core"), None)
    return jax.shard_map(
        per_device,
        mesh=split,
        in_specs=(rows, rows, rows, rows, rows, P("member", None, None)),
        out_specs=(rows, rows, rows, rows),
        check_vma=False,
    )
```

```python
import functools
import math

import jax
import jax.numpy as jnp
from jax import lax
from jax.experimental import pallas as pl
from jax.experimental.pallas import tpu as pltpu
from jax.sharding import Mesh
from jax.sharding import PartitionSpec as P

HEADS = 20
HSIZE = 128
BLK = 64
QBLK = 16
NSEL = 6
LEN = 1024

SLOT_XOR = (0, 2, 1, 3)


def masked_scores(q, k, mask):
    scaling = 1.0 / math.sqrt(HSIZE)
    nt = (((1,), (1,)), ((), ()))
    s = lax.dot_general(q, k, nt, preferred_element_type=jnp.float32) * scaling
    return jnp.where(mask > 0, s, -jnp.inf)


def fwd_kernel(q_ref, k0, k1, k2, k3, v0, v1, v2, v3, mask_ref, ctx_ref, lse_ref):
    mask = mask_ref[...]
    for h in range(lse_ref.shape[0]):
        cols = slice(h * HSIZE, (h + 1) * HSIZE)
        q = q_ref[:, cols]
        k = jnp.concatenate([k0[:, cols], k1[:, cols], k2[:, cols], k3[:, cols]], axis=0)
        v = jnp.concatenate([v0[:, cols], v1[:, cols], v2[:, cols], v3[:, cols]], axis=0)
        s = masked_scores(q, k, mask)
        m = jnp.max(s, axis=1, keepdims=True)
        e = jnp.exp(s - m)
        total = jnp.sum(e, axis=1, keepdims=True)
        lse = m + jnp.log(total)
        p_low = (e * (1.0 / total)).astype(jnp.bfloat16)
        ctx = jnp.dot(p_low, v, preferred_element_type=jnp.float32)
        ctx_ref[:, cols] = ctx.astype(jnp.bfloat16)
        lse_ref[h] = lse


def bwd_kernel(q_ref, k0, k1, k2, k3, v0, v1, v2, v3, do_ref, ctx_ref, lse_ref, mask_ref,
               dq_ref, dk_keep, dk_send, dv_keep, dv_send):
    scaling = 1.0 / math.sqrt(HSIZE)
    nt = (((1,), (1,)), ((), ()))
    tn = (((0,), (0,)), ((), ()))
    mask = mask_ref[...]
    for h in range(lse_ref.shape[0]):
        cols = slice(h * HSIZE, (h + 1) * HSIZE)
        q = q_ref[:, cols]
        k = jnp.concatenate([k0[:, cols], k1[:, cols], k2[:, cols], k3[:, cols]], axis=0)
        v = jnp.concatenate([v0[:, cols], v1[:, cols], v2[:, cols], v3[:, cols]], axis=0)
        s = masked_scores(q, k, mask)
        p = jnp.exp(s - lse_ref[h])
        p_low = p.astype(jnp.bfloat16)
        do = do_ref[:, cols]
        dp = lax.dot_general(do, v, nt, preferred_element_type=jnp.float32)
        delta = jnp.sum(
            do.astype(jnp.float32) * ctx_ref[:, cols].astype(jnp.float32), axis=1, keepdims=True
        )
        ds = (p * (dp - delta)).astype(jnp.bfloat16)
        dq = jnp.dot(ds, k, preferred_element_type=jnp.float32) * scaling
        dq_ref[:, cols] = dq.astype(jnp.bfloat16)
        dk = lax.dot_general(ds, q, tn, preferred_element_type=jnp.float32) * scaling
        dv = lax.dot_general(p_low, do, tn, preferred_element_type=jnp.float32)
        dk = dk.astype(jnp.bfloat16).reshape(4, -1, HSIZE)
        dv = dv.astype(jnp.bfloat16).reshape(4, -1, HSIZE)
        dk_keep[:, :, cols] = dk[0:2]
        dk_send[:, :, cols] = dk[2:4]
        dv_keep[:, :, cols] = dv[0:2]
        dv_send[:, :, cols] = dv[2:4]


def attention_fwd(q, ks, vs, mask, per_step):
    rows, width = q.shape
    heads = width // HSIZE
    col = pl.BlockSpec((rows, per_step * HSIZE), lambda h: (0, h))
    return pl.pallas_call(
        fwd_kernel,
        grid=(heads // per_step,),
        cost_estimate=pl.CostEstimate(
            flops=heads * 2 * 10**9, transcendentals=heads * rows * 1024,
            bytes_accessed=12 * rows * width * 2,
        ),
        in_specs=[col] * 9 + [pl.BlockSpec(mask.shape, lambda h: (0, 0))],
        out_specs=[col, pl.BlockSpec((per_step, rows, 1), lambda h: (h, 0, 0))],
        out_shape=[
            jax.ShapeDtypeStruct((rows, width), jnp.bfloat16),
            jax.ShapeDtypeStruct((heads, rows, 1), jnp.float32),
        ],
    )(q, *ks, *vs, mask)


def attention_bwd(q, ks, vs, do, ctx, lse, mask, first, count, per_step):
    rows, width = q.shape
    lead = first // per_step
    span = per_step * HSIZE
    col = pl.BlockSpec((rows, span), lambda h: (0, h + lead))
    out_col = pl.BlockSpec((rows, span), lambda h: (0, h))
    slot_col = pl.BlockSpec((2, rows, span), lambda h: (0, 0, h))
    return pl.pallas_call(
        bwd_kernel,
        grid=(count // per_step,),
        cost_estimate=pl.CostEstimate(
            flops=count * 14 * 10**8, transcendentals=count * rows * 1024,
            bytes_accessed=12 * rows * width,
        ),
        in_specs=[col] * 9
        + [out_col, col]
        + [
            pl.BlockSpec((per_step, rows, 1), lambda h: (h + lead, 0, 0)),
            pl.BlockSpec(mask.shape, lambda h: (0, 0)),
        ],
        out_specs=[out_col] + [slot_col] * 4,
        out_shape=[jax.ShapeDtypeStruct((rows, count * HSIZE), jnp.bfloat16)]
        + [jax.ShapeDtypeStruct((2, rows, count * HSIZE), jnp.bfloat16)] * 4,
    )(q, *ks, *vs, do, ctx, lse, mask)


def swap(x, axis):
    count = lax.axis_size(axis)
    return lax.ppermute(x, axis, [(i, i ^ 1) for i in range(count)])


def per_device(query_rows, key_rows, value_rows, weight_out, cotangent, pattern):
    tok_rows = query_rows.shape[0]
    blocks_here = tok_rows // BLK
    zpos = lax.axis_index("z")
    ypos = lax.axis_index("y")
    core = lax.axis_index("core")
    seq_shards = LEN // tok_rows
    position = (ypos % 2) * 2 + core
    sequence = zpos * (lax.axis_size("y") // 2) + ypos // 2

    full_weight = lax.all_gather(weight_out, ("z", "y", "core"), axis=0, tiled=True)

    k_x = swap(key_rows, "y")
    v_x = swap(value_rows, "y")
    k_p = swap(key_rows, "core")
    v_p = swap(value_rows, "core")
    k_d = swap(k_x, "core")
    v_d = swap(v_x, "core")

    seq_plan = lax.dynamic_index_in_dim(pattern, sequence, 0, keepdims=False)
    own_plan = lax.dynamic_slice_in_dim(seq_plan, position * blocks_here, blocks_here, 0)
    rel = jnp.arange(seq_shards * tok_rows, dtype=jnp.int32) // BLK
    slot_xor = jnp.array(SLOT_XOR, dtype=jnp.int32)[rel // blocks_here]
    key_block = (position ^ slot_xor) * blocks_here + rel % blocks_here
    plan_rows = own_plan[jnp.arange(tok_rows, dtype=jnp.int32) // BLK]
    hits = [plan_rows[:, j][:, None] == key_block[None, :] for j in range(NSEL)]
    mask = functools.reduce(jnp.logical_or, hits).astype(jnp.float32)

    ks = (key_rows, k_x, k_p, k_d)
    vs = (value_rows, v_x, v_p, v_d)
    ctx, lse = attention_fwd(query_rows, ks, vs, mask, 4)


    def presum(keep, send):
        back = swap(send, "core")
        own = keep[0].astype(jnp.float32) + back[0].astype(jnp.float32)
        cross = (keep[1].astype(jnp.float32) + back[1].astype(jnp.float32)).astype(jnp.bfloat16)
        return own, cross

    def finish(own, cross):
        arrived = swap(cross, "y")
        return (own + arrived.astype(jnp.float32)).astype(jnp.bfloat16)

    heads = query_rows.shape[1] // HSIZE
    half = heads // 2
    pieces = []
    later = (query_rows, ctx)
    for first, count in ((0, half), (half, heads - half)):
        q_in, ctx_in = later
        w_rows = lax.slice_in_dim(full_weight, first * HSIZE, (first + count) * HSIZE, axis=0)
        do_part = lax.dot_general(
            cotangent, w_rows, (((1,), (1,)), ((), ())), preferred_element_type=jnp.float32
        ).astype(jnp.bfloat16)
        dq, dk_keep, dk_send, dv_keep, dv_send = attention_bwd(
            q_in, ks, vs, do_part, ctx_in, lse, mask, first, count, 5
        )
        k_own, k_cross = presum(dk_keep, dk_send)
        v_own, v_cross = presum(dv_keep, dv_send)
        later, k_cross, v_cross = lax.optimization_barrier((later, k_cross, v_cross))
        pieces.append((dq, finish(k_own, k_cross), finish(v_own, v_cross)))
    grad_queries = jnp.concatenate([p[0] for p in pieces], axis=1)
    grad_keys = jnp.concatenate([p[1] for p in pieces], axis=1)
    grad_values = jnp.concatenate([p[2] for p in pieces], axis=1)

    ctx_out = later[1]
    sublayer_out = jnp.dot(ctx_out, full_weight, preferred_element_type=jnp.float32).astype(
        jnp.bfloat16
    )
    return (sublayer_out, grad_queries, grad_keys, grad_values)


def solution(mesh):
    devices = mesh.devices.reshape(mesh.devices.shape[0], -1, 4, 2)
    split = Mesh(devices, ("member", "z", "y", "core"))
    rows = P(("member", "z", "y", "core"), None)
    return jax.shard_map(
        per_device,
        mesh=split,
        in_specs=(rows, rows, rows, rows, rows, P("member", None, None)),
        out_specs=(rows, rows, rows, rows),
        check_vma=False,
    )
```
